256 devices in a mesh: leaf: 4 (over y), row: 8 (over z), col: 8 (over x, core).
Axes of the slice: x: 4, y: 4, z: 8, core: 2. Of those that a mesh axis runs over, the one named last changes fastest.
Arguments:
- rhs: float32 [4, 4, 8, 256, 256], P('leaf', None, 'row'), may hold values from -6 to 6
- rhs_top: float32 [2, 8, 256, 256], P(None, 'row'), may hold values from -6 to 6
- factor: bfloat16 [4, 4, 8, 4, 8, 256, 256], P('leaf', None, 'row', None, 'col'), may hold values from -0.125 to 0.125
- factor_inv: bfloat16 [4, 2, 4, 8, 256, 256], P('leaf', None, None, 'row')
- lower_bridge: bfloat16 [4, 2, 8, 4, 8, 256, 256], P('leaf', None, 'row', None, 'col'), may hold values from -0.0625 to 0.0625
- upper_bridge: bfloat16 [4, 4, 8, 2, 8, 256, 256], P('leaf', None, 'row', None, 'col'), may hold values from -0.1875 to 0.1875
- top_factor: bfloat16 [2, 8, 2, 8, 256, 256], P(None, 'row', None, 'col'), may hold values from -0.1875 to 0.1875
- top_inv: bfloat16 [2, 2, 8, 256, 256], P(None, None, 'row')
- widths: int32 [4, 4, 8], P('leaf', None, 'row'), may hold values from 128 to 256, as said below
- pattern: int32 [4, 4, 8, 4, 8], P('leaf', None, 'row', None, 'col'), may hold values 0 or 1
- lower_links: int32 [4, 2, 8, 4, 8], P('leaf', None, 'row', None, 'col'), may hold values 0 or 1
- upper_links: int32 [4, 4, 8, 2, 8], P('leaf', None, 'row', None, 'col'), may hold values 0 or 1
- top_pattern: int32 [2, 8, 2, 8], P(None, 'row', None, 'col'), may hold values 0 or 1
Outputs:
- solution: float32 [4, 4, 8, 256, 256], P('leaf', None, 'row', None, 'col')
- solution_top: float32 [2, 8, 256, 256], P(None, 'row', None, 'col')
The draws below stay inside these ranges and needn't reach their ends.
Inputs may be any that keep to these rules, and one draw needn't show every extreme that they name: widths of supernodes; the largest is 256 in every subtree.
All inputs are finite; a program needn't handle non-finite values. No bound on the sum of `pattern` or of `lower_links` or of `upper_links` or of `top_pattern` on one device may be relied on, other than what follows from the above.
Results may differ from the reference program's by a relative error of at most 0.02.
Values may be sent and summed in bfloat16 or wider, within the bound.
No kernel may reach another device: no remote copies, remote signals or barrier semaphores. Data moves between devices by JAX's collectives and lax.ppermute only.
A program may use at most 64 MiB of HBM per device.

```python
import jax
import jax.numpy as jnp

B = 256
R = 256
S = 8
LEV = 4
TOP = 2
LEAVES = 4


def inverse_blocks(key, shape):
    eye = jnp.eye(B, dtype=jnp.float32)
    noise = jax.random.normal(key, shape, jnp.float32)
    return eye + noise * (0.5 / B ** 0.5)


def draw_factor_inv(key, part):
    return inverse_blocks(jax.random.fold_in(key, 11), (LEAVES, 2, LEV, S, B, B)).astype(jnp.bfloat16)


def draw_top_inv(key, part):
    return inverse_blocks(jax.random.fold_in(key, 13), (2, TOP, S, B, B)).astype(jnp.bfloat16)


def draw_widths(key, part):
    base = jax.random.randint(jax.random.fold_in(key, 17), (LEAVES, LEV * S), B // 2, B + 1)
    spot = jax.random.randint(jax.random.fold_in(key, 19), (LEAVES, 1), 0, LEV * S)
    places = jnp.arange(LEV * S, dtype=jnp.int32)[None, :]
    full = jnp.where(places == spot, B, base)
    return full.reshape(LEAVES, LEV, S).astype(jnp.int32)


def set_ends(array, key, low, top_value):
    dims = array.shape
    index_at = [jax.random.randint(jax.random.fold_in(key, axis), (), 0, dims[axis]) for axis in range(len(dims))]
    array = array.at[tuple(index_at)].set(low)
    longest = dims.index(max(dims))
    index_at[longest] = (index_at[longest] + 1) % dims[longest]
    return array.at[tuple(index_at)].set(top_value)


def steps_of(key, dims, shards, low, top_value):
    level, own = 1.0, jax.random.fold_in(key, 6)
    for position, parts in shards:
        draws = jnp.exp(jax.random.uniform(jax.random.fold_in(own, position), (parts,), jnp.float32, low / len(shards), top_value / len(shards)))
        level = level * jnp.repeat(draws, dims[position] // parts).reshape([-1 if axis == position else 1 for axis in range(len(dims))])
    return level


def scatter_about(key, extent, width, reach, cuts=(), held_as=jnp.bfloat16):
    result = jax.random.normal(key, extent, jnp.float32) * width
    if len(cuts) > 0:
        result = steps_of(key, extent, cuts, -0.22, 0.18) * result
    return jnp.clip(result, min=-reach, max=reach).astype(held_as)


def setup_inputs(seed: int = 0) -> dict:
    seeds = jax.random.split(jax.random.key(seed), 14)
    rhs = scatter_about(seeds[0], (LEAVES, LEV, S, B, R), 1.0, 6.0, ((0, 4), (2, 8)), jnp.float32)
    rhs_top = scatter_about(seeds[1], (TOP, S, B, R), 1.0, 6.0, ((1, 8),), jnp.float32)
    factor = scatter_about(seeds[2], (LEAVES, LEV, S, LEV, S, B, B), (B * S) ** -0.5, 0.125, ((0, 4), (2, 8), (4, 8)))
    factor_inv = draw_factor_inv(jax.random.fold_in(seeds[13], 71), 0)
    lower_bridge = scatter_about(seeds[4], (LEAVES, TOP, S, LEV, S, B, B), (B * S * LEV * LEAVES // 4) ** -0.5, 0.0625, ((0, 4), (2, 8), (4, 8)))
    upper_bridge = scatter_about(seeds[5], (LEAVES, LEV, S, TOP, S, B, B), (B * S * TOP // 4) ** -0.5, 0.1875, ((0, 4), (2, 8), (4, 8)))
    top_factor = scatter_about(seeds[6], (TOP, S, TOP, S, B, B), (B * S // 2) ** -0.5, 0.1875, ((1, 8), (3, 8)))
    top_inv = draw_top_inv(jax.random.fold_in(seeds[13], 71), 0)
    widths = draw_widths(jax.random.fold_in(seeds[13], 71), 0)
    pattern = set_ends((jax.random.randint(seeds[9], (LEAVES, LEV, S, LEV, S), 0, 3) < 2).astype(jnp.int32), jax.random.fold_in(seeds[9], 1), 0, 1)
    lower_links = set_ends((jax.random.randint(seeds[10], (LEAVES, TOP, S, LEV, S), 0, 3) < 2).astype(jnp.int32), jax.random.fold_in(seeds[10], 1), 0, 1)
    upper_links = set_ends((jax.random.randint(seeds[11], (LEAVES, LEV, S, TOP, S), 0, 3) < 2).astype(jnp.int32), jax.random.fold_in(seeds[11], 1), 0, 1)
    top_pattern = set_ends((jax.random.randint(seeds[12], (TOP, S, TOP, S), 0, 3) < 2).astype(jnp.int32), jax.random.fold_in(seeds[12], 1), 0, 1)
    return dict(rhs=rhs, rhs_top=rhs_top, factor=factor, factor_inv=factor_inv, lower_bridge=lower_bridge, upper_bridge=upper_bridge, top_factor=top_factor, top_inv=top_inv, widths=widths, pattern=pattern, lower_links=lower_links, upper_links=upper_links, top_pattern=top_pattern)


def masked(blocks, marks):
    return blocks * marks.astype(jnp.bfloat16)[..., None, None]


def reference(rhs, rhs_top, factor, factor_inv, lower_bridge, upper_bridge, top_factor, top_inv, widths, pattern, lower_links, upper_links, top_pattern):
    f32 = jnp.float32
    bf16 = jnp.bfloat16
    fmask = masked(factor, pattern)
    lmask = masked(lower_bridge, lower_links)
    umask = masked(upper_bridge, upper_links)
    tmask = masked(top_factor, top_pattern)
    keep = (jnp.arange(B, dtype=jnp.int32)[None, None, None, :] < widths[..., None]).astype(f32)[..., None]
    ys = []
    segs = []
    for level in range(LEV):
        if level == 0:
            summed = jnp.zeros((LEAVES, S, B, R), f32)
        else:
            summed = jnp.einsum('giljbk,gljkr->gibr', fmask[:, level, :, :level].astype(f32), jnp.stack(segs, 1).astype(f32))
        resid = (rhs[:, level] - summed).astype(bf16)
        solved = keep[:, level] * jnp.einsum('gibk,gikr->gibr', factor_inv[:, 0, level].astype(f32), resid.astype(f32))
        ys.append(solved)
        segs.append(solved.astype(bf16))
    seg_all = jnp.stack(segs, 1).astype(f32)
    couple = []
    for top in range(TOP):
        couple.append(jnp.einsum('giljbk,gljkr->ibr', lmask[:, top].astype(f32), seg_all))
    yts = []
    tsegs = []
    for top in range(TOP):
        summed = couple[top]
        if top > 0:
            summed = summed + jnp.einsum('iljbk,ljkr->ibr', tmask[top, :, :top].astype(f32), jnp.stack(tsegs, 0).astype(f32))
        resid = (rhs_top[top] - summed).astype(bf16)
        solved = jnp.einsum('ibk,ikr->ibr', top_inv[0, top].astype(f32), resid.astype(f32))
        yts.append(solved)
        tsegs.append(solved.astype(bf16))
    zts = [None] * TOP
    tback = [None] * TOP
    for top in reversed(range(TOP)):
        if top == TOP - 1:
            summed = jnp.zeros((S, B, R), f32)
        else:
            summed = jnp.einsum('iljbk,ljkr->ibr', tmask[top, :, top + 1:].astype(f32), jnp.stack(tback[top + 1:], 0).astype(f32))
        resid = (yts[top] - summed).astype(bf16)
        solved = jnp.einsum('ibk,ikr->ibr', top_inv[1, top].astype(f32), resid.astype(f32))
        zts[top] = solved
        tback[top] = solved.astype(bf16)
    top_stack = jnp.stack(tback, 0).astype(f32)
    zs = [None] * LEV
    back = [None] * LEV
    for level in reversed(range(LEV)):
        summed = jnp.einsum('gitjbk,tjkr->gibr', umask[:, level].astype(f32), top_stack)
        if level < LEV - 1:
            summed = summed + jnp.einsum('giljbk,gljkr->gibr', fmask[:, level, :, level + 1:].astype(f32), jnp.stack(back[level + 1:], 1).astype(f32))
        resid = (ys[level] - summed).astype(bf16)
        solved = keep[:, level] * jnp.einsum('gibk,gikr->gibr', factor_inv[:, 1, level].astype(f32), resid.astype(f32))
        zs[level] = solved
        back[level] = solved.astype(bf16)
    return jnp.stack(zs, 1), jnp.stack(zts, 0)
```

```python
import jax
import jax.numpy as jnp
from jax import lax
from jax.sharding import PartitionSpec as P

GRID = ("row", "col")


def masked(blocks, marks):
    return blocks * marks.astype(jnp.bfloat16)[..., None, None]


def tree_sum(parts):
    while len(parts) > 1:
        parts = [parts[i] + parts[i + 1] for i in range(0, len(parts), 2)]
    return parts[0]


def to_columns(x, n):
    pairs = [(r * n + c, c * n + r) for r in range(n) for c in range(n)]
    return lax.ppermute(x, GRID, pairs)


def row_sum_on_columns(part, n):
    got = []
    for k in range(n):
        pairs = [(r * n + c, (c ^ k) * n + r) for r in range(n) for c in range(n)]
        got.append(lax.ppermute(part, GRID, pairs))
    return tree_sum(got)


def leaf_sum(x, n):
    got = [x] + [lax.ppermute(x, "leaf", [(g, g ^ k) for g in range(n)]) for k in range(1, n)]
    return tree_sum(got)


def products(blocks, segments):
    return jnp.einsum(
        "jbk,jkr->br", jnp.stack(blocks, 0), jnp.stack(segments, 0), preferred_element_type=jnp.float32
    )


def shards(
    rhs,
    rhs_top,
    factor,
    factor_inv,
    lower_bridge,
    upper_bridge,
    top_factor,
    top_inv,
    widths,
    pattern,
    lower_links,
    upper_links,
    top_pattern,
):
    f32 = jnp.float32
    bf16 = jnp.bfloat16
    n = lax.axis_size("row")
    leaves = lax.axis_size("leaf")
    levels = factor.shape[1]
    tops = top_factor.shape[0]
    block = factor.shape[5]
    sides = rhs.shape[4]
    share = sides // n

    fm = masked(factor[0, :, 0, :, 0], pattern[0, :, 0, :, 0])
    lm = masked(lower_bridge[0, :, 0, :, 0], lower_links[0, :, 0, :, 0])
    um = masked(upper_bridge[0, :, 0, :, 0], upper_links[0, :, 0, :, 0])
    tm = masked(top_factor[:, 0, :, 0], top_pattern[:, 0, :, 0])
    marks = lax.broadcasted_iota(jnp.int32, (levels, block, 1), 1)
    keep_own = (marks < widths[0, :, 0][:, None, None]).astype(f32)
    rhs_own = rhs[0, :, 0]
    inv_own = factor_inv[0, :, :, 0]

    seg0_own = (
        keep_own[0] * jnp.dot(inv_own[0, 0], rhs_own[0].astype(bf16), preferred_element_type=f32)
    ).astype(bf16)
    seg0 = to_columns(seg0_own, n)

    rhs_b = to_columns(rhs_own, n)
    inv_b = to_columns(inv_own, n)
    keep_b = to_columns(keep_own, n)
    top_rhs_b = to_columns(rhs_top[:, 0], n)
    top_inv_b = to_columns(top_inv[:, :, 0], n)

    ys = [keep_b[0] * jnp.dot(inv_b[0, 0], rhs_b[0].astype(bf16), preferred_element_type=f32)]
    segs = [seg0]
    for level in range(1, levels):
        part = products([fm[level, j] for j in range(level)], segs)
        full = row_sum_on_columns(part, n)
        resid = (rhs_b[level] - full).astype(bf16)
        solved = keep_b[level] * jnp.dot(inv_b[0, level], resid, preferred_element_type=f32)
        ys.append(solved)
        segs.append(solved.astype(bf16))

    coupling = jnp.stack([products([lm[t, j] for j in range(levels)], segs) for t in range(tops)], 0)
    coupling = leaf_sum(coupling, leaves)

    yts = []
    tsegs = []
    for top in range(tops):
        part = coupling[top]
        if top > 0:
            part = part + products([tm[top, j] for j in range(top)], tsegs)
        full = row_sum_on_columns(part, n)
        resid = (top_rhs_b[top] - full).astype(bf16)
        solved = jnp.dot(top_inv_b[0, top], resid, preferred_element_type=f32)
        yts.append(solved)
        tsegs.append(solved.astype(bf16))

    zts = [None] * tops
    tback = [None] * tops
    for top in reversed(range(tops)):
        if top == tops - 1:
            resid = yts[top].astype(bf16)
        else:
            part = products([tm[top, j] for j in range(top + 1, tops)], tback[top + 1 :])
            full = row_sum_on_columns(part, n)
            resid = (yts[top] - full).astype(bf16)
        solved = jnp.dot(top_inv_b[1, top], resid, preferred_element_type=f32)
        zts[top] = solved
        tback[top] = solved.astype(bf16)

    zs = [None] * levels
    back = [None] * levels
    for level in reversed(range(levels)):
        blocks = [um[level, t] for t in range(tops)] + [fm[level, j] for j in range(level + 1, levels)]
        part = products(blocks, tback + back[level + 1 :])
        full = row_sum_on_columns(part, n)
        resid = (ys[level] - full).astype(bf16)
        solved = keep_b[level] * jnp.dot(inv_b[1, level], resid, preferred_element_type=f32)
        zs[level] = solved
        back[level] = solved.astype(bf16)

    start = lax.axis_index("row") * share
    chunks = [lax.dynamic_slice_in_dim(z, start, share, 1) for z in zs]
    top_chunks = [lax.dynamic_slice_in_dim(z, start, share, 1) for z in zts]
    result = jnp.stack([to_columns(c, n) for c in chunks], 0)
    result_top = jnp.stack([to_columns(c, n) for c in top_chunks], 0)
    return (result[None, :, None], result_top[:, None])


def solution(mesh):
    assert mesh.shape["row"] == mesh.shape["col"]
    placed = (
        P("leaf", None, "row", None, None),
        P(None, "row", None, None),
        P("leaf", None, "row", None, "col", None, None),
        P("leaf", None, None, "row", None, None),
        P("leaf", None, "row", None, "col", None, None),
        P("leaf", None, "row", None, "col", None, None),
        P(None, "row", None, "col", None, None),
        P(None, None, "row", None, None),
        P("leaf", None, "row"),
        P("leaf", None, "row", None, "col"),
        P("leaf", None, "row", None, "col"),
        P("leaf", None, "row", None, "col"),
        P(None, "row", None, "col"),
    )
    return jax.shard_map(
        shards,
        mesh=mesh,
        in_specs=placed,
        out_specs=(P("leaf", None, "row", None, "col"), P(None, "row", None, "col")),
        check_vma=False,
    )
```

```python
import jax
import jax.numpy as jnp
from jax import lax
from jax.sharding import PartitionSpec as P

GRID = ("row", "col")


def masked(blocks, marks):
    return blocks * marks.astype(jnp.bfloat16)[..., None, None]


def to_columns(x, n):
    pairs = [(r * n + c, c * n + r) for r in range(n) for c in range(n)]
    return lax.ppermute(x, GRID, pairs)


def butterfly(x, axis, n):
    k = 1
    while k < n:
        x = x + lax.ppermute(x, axis, [(i, i ^ k) for i in range(n)])
        k *= 2
    return x


def products(blocks, segments):
    return jnp.einsum(
        "jbk,jkr->br", jnp.stack(blocks, 0), jnp.stack(segments, 0), preferred_element_type=jnp.float32
    )


def shards(
    rhs,
    rhs_top,
    factor,
    factor_inv,
    lower_bridge,
    upper_bridge,
    top_factor,
    top_inv,
    widths,
    pattern,
    lower_links,
    upper_links,
    top_pattern,
):
    f32 = jnp.float32
    bf16 = jnp.bfloat16
    n = lax.axis_size("row")
    ncol = lax.axis_size("col")
    leaves = lax.axis_size("leaf")
    levels = factor.shape[1]
    tops = top_factor.shape[0]
    block = factor.shape[5]
    sides = rhs.shape[4]
    share = sides // ncol

    fm = masked(factor[0, :, 0, :, 0], pattern[0, :, 0, :, 0])
    lm = masked(lower_bridge[0, :, 0, :, 0], lower_links[0, :, 0, :, 0])
    um = masked(upper_bridge[0, :, 0, :, 0], upper_links[0, :, 0, :, 0])
    tm = masked(top_factor[:, 0, :, 0], top_pattern[:, 0, :, 0])
    marks = lax.broadcasted_iota(jnp.int32, (levels, block, 1), 1)
    keep = (marks < widths[0, :, 0][:, None, None]).astype(f32)
    own_rhs = rhs[0, :, 0]
    inv = factor_inv[0, :, :, 0]
    top_rhs = rhs_top[:, 0]
    tinv = top_inv[:, :, 0]

    ys = []
    segs = []
    for level in range(levels):
        if level == 0:
            resid = own_rhs[0].astype(bf16)
        else:
            part = products([fm[level, j] for j in range(level)], segs)
            resid = (own_rhs[level] - butterfly(part, "col", ncol)).astype(bf16)
        solved = keep[level] * jnp.dot(inv[0, level], resid, preferred_element_type=f32)
        ys.append(solved)
        segs.append(to_columns(solved.astype(bf16), n))

    coupling = jnp.stack([products([lm[t, j] for j in range(levels)], segs) for t in range(tops)], 0)
    coupling = butterfly(butterfly(coupling, "col", ncol), "leaf", leaves)

    yts = []
    tsegs = []
    for top in range(tops):
        summed = coupling[top]
        if top > 0:
            part = products([tm[top, j] for j in range(top)], tsegs)
            summed = summed + butterfly(part, "col", ncol)
        resid = (top_rhs[top] - summed).astype(bf16)
        solved = jnp.dot(tinv[0, top], resid, preferred_element_type=f32)
        yts.append(solved)
        tsegs.append(to_columns(solved.astype(bf16), n))

    zts = [None] * tops
    tback = [None] * tops
    for top in reversed(range(tops)):
        if top == tops - 1:
            resid = yts[top].astype(bf16)
        else:
            part = products([tm[top, j] for j in range(top + 1, tops)], tback[top + 1 :])
            resid = (yts[top] - butterfly(part, "col", ncol)).astype(bf16)
        solved = jnp.dot(tinv[1, top], resid, preferred_element_type=f32)
        zts[top] = solved
        tback[top] = to_columns(solved.astype(bf16), n)

    zs = [None] * levels
    back = [None] * levels
    for level in reversed(range(levels)):
        blocks = [um[level, t] for t in range(tops)] + [fm[level, j] for j in range(level + 1, levels)]
        part = products(blocks, tback + back[level + 1 :])
        resid = (ys[level] - butterfly(part, "col", ncol)).astype(bf16)
        solved = keep[level] * jnp.dot(inv[1, level], resid, preferred_element_type=f32)
        zs[level] = solved
        if level > 0:
            back[level] = to_columns(solved.astype(bf16), n)

    start = lax.axis_index("col") * share
    result = lax.dynamic_slice_in_dim(jnp.stack(zs, 0), start, share, 2)
    result_top = lax.dynamic_slice_in_dim(jnp.stack(zts, 0), start, share, 2)
    return (result[None, :, None], result_top[:, None])


def solution(mesh):
    assert mesh.shape["row"] == mesh.shape["col"]
    placed = (
        P("leaf", None, "row", None, None),
        P(None, "row", None, None),
        P("leaf", None, "row", None, "col", None, None),
        P("leaf", None, None, "row", None, None),
        P("leaf", None, "row", None, "col", None, None),
        P("leaf", None, "row", None, "col", None, None),
        P(None, "row", None, "col", None, None),
        P(None, None, "row", None, None),
        P("leaf", None, "row"),
        P("leaf", None, "row", None, "col"),
        P("leaf", None, "row", None, "col"),
        P("leaf", None, "row", None, "col"),
        P(None, "row", None, "col"),
    )
    return jax.shard_map(
        shards,
        mesh=mesh,
        in_specs=placed,
        out_specs=(P("leaf", None, "row", None, "col"), P(None, "row", None, "col")),
        check_vma=False,
    )
```

```python
import jax
import jax.numpy as jnp
from jax import lax
from jax.sharding import PartitionSpec as P

GRID = ("row", "col")


def masked(blocks, marks):
    return blocks * marks.astype(jnp.bfloat16)[..., None, None]


def ring_distance(a, b, size):
    d = abs(a - b) % size
    return min(d, size - d)


def to_columns(x, n):
    pairs = []
    for c in range(n):
        targets = sorted(range(n), key=lambda r: (-ring_distance(r, c, n), r))
        sources = sorted(range(n), key=lambda s: (ring_distance(s // 2, c // 2, n // 2), s % 2 != c % 2, s))
        pairs += [(c * n + s, r * n + c) for r, s in zip(targets, sources)]
    return lax.ppermute(x, GRID, pairs)


def tree_sum(parts):
    while len(parts) > 1:
        parts = [parts[i] + parts[i + 1] for i in range(0, len(parts), 2)]
    return parts[0]


def group_sum(x, axis, n, step=1):
    got = [x] + [lax.ppermute(x, axis, [(i, i ^ (step * k)) for i in range(n)]) for k in range(1, n // step)]
    return tree_sum(got)


def column_total(x, n):
    x = x + lax.ppermute(x, "col", [(i, i ^ 1) for i in range(n)])
    return group_sum(x, "col", n, 2)


def products(blocks, segments):
    return jnp.einsum(
        "jbk,jkr->br", jnp.stack(blocks, 0), jnp.stack(segments, 0), preferred_element_type=jnp.float32
    )


def shards(
    rhs,
    rhs_top,
    factor,
    factor_inv,
    lower_bridge,
    upper_bridge,
    top_factor,
    top_inv,
    widths,
    pattern,
    lower_links,
    upper_links,
    top_pattern,
):
    f32 = jnp.float32
    bf16 = jnp.bfloat16
    n = lax.axis_size("row")
    ncol = lax.axis_size("col")
    leaves = lax.axis_size("leaf")
    levels = factor.shape[1]
    tops = top_factor.shape[0]
    block = factor.shape[5]
    sides = rhs.shape[4]
    share = sides // ncol

    fm = masked(factor[0, :, 0, :, 0], pattern[0, :, 0, :, 0])
    lm = masked(lower_bridge[0, :, 0, :, 0], lower_links[0, :, 0, :, 0])
    um = masked(upper_bridge[0, :, 0, :, 0], upper_links[0, :, 0, :, 0])
    tm = masked(top_factor[:, 0, :, 0], top_pattern[:, 0, :, 0])
    marks = lax.broadcasted_iota(jnp.int32, (levels, block, 1), 1)
    keep = (marks < widths[0, :, 0][:, None, None]).astype(f32)
    own_rhs = rhs[0, :, 0]
    inv = factor_inv[0, :, :, 0]
    top_rhs = rhs_top[:, 0]
    tinv = top_inv[:, :, 0]

    ys = []
    segs = []
    for level in range(levels):
        if level == 0:
            resid = own_rhs[0].astype(bf16)
        else:
            part = products([fm[level, j] for j in range(level)], segs)
            resid = (own_rhs[level] - column_total(part, ncol)).astype(bf16)
        solved = keep[level] * jnp.dot(inv[0, level], resid, preferred_element_type=f32)
        ys.append(solved)
        segs.append(to_columns(solved.astype(bf16), n))

    coupling = jnp.stack([products([lm[t, j] for j in range(levels)], segs) for t in range(tops)], 0)
    coupling = group_sum(column_total(coupling, ncol), "leaf", leaves)

    yts = []
    tsegs = []
    for top in range(tops):
        summed = coupling[top]
        if top > 0:
            part = products([tm[top, j] for j in range(top)], tsegs)
            summed = summed + column_total(part, ncol)
        resid = (top_rhs[top] - summed).astype(bf16)
        solved = jnp.dot(tinv[0, top], resid, preferred_element_type=f32)
        yts.append(solved)
        tsegs.append(to_columns(solved.astype(bf16), n))

    zts = [None] * tops
    tback = [None] * tops
    for top in reversed(range(tops)):
        if top == tops - 1:
            resid = yts[top].astype(bf16)
        else:
            part = products([tm[top, j] for j in range(top + 1, tops)], tback[top + 1 :])
            resid = (yts[top] - column_total(part, ncol)).astype(bf16)
        solved = jnp.dot(tinv[1, top], resid, preferred_element_type=f32)
        zts[top] = solved
        tback[top] = to_columns(solved.astype(bf16), n)

    zs = [None] * levels
    back = [None] * levels
    for level in reversed(range(levels)):
        blocks = [um[level, t] for t in range(tops)] + [fm[level, j] for j in range(level + 1, levels)]
        part = products(blocks, tback + back[level + 1 :])
        resid = (ys[level] - column_total(part, ncol)).astype(bf16)
        solved = keep[level] * jnp.dot(inv[1, level], resid, preferred_element_type=f32)
        zs[level] = solved
        if level > 0:
            back[level] = to_columns(solved.astype(bf16), n)

    start = lax.axis_index("col") * share
    result = lax.dynamic_slice_in_dim(jnp.stack(zs, 0), start, share, 2)
    result_top = lax.dynamic_slice_in_dim(jnp.stack(zts, 0), start, share, 2)
    return (result[None, :, None], result_top[:, None])


def solution(mesh):
    assert mesh.shape["row"] == mesh.shape["col"]
    placed = (
        P("leaf", None, "row", None, None),
        P(None, "row", None, None),
        P("leaf", None, "row", None, "col", None, None),
        P("leaf", None, None, "row", None, None),
        P("leaf", None, "row", None, "col", None, None),
        P("leaf", None, "row", None, "col", None, None),
        P(None, "row", None, "col", None, None),
        P(None, None, "row", None, None),
        P("leaf", None, "row"),
        P("leaf", None, "row", None, "col"),
        P("leaf", None, "row", None, "col"),
        P("leaf", None, "row", None, "col"),
        P(None, "row", None, "col"),
    )
    return jax.shard_map(
        shards,
        mesh=mesh,
        in_specs=placed,
        out_specs=(P("leaf", None, "row", None, "col"), P(None, "row", None, "col")),
        check_vma=False,
    )
```

```python
import jax
import jax.numpy as jnp
from jax import lax
from jax.sharding import PartitionSpec as P

GRID = ("row", "col")


def masked(blocks, marks):
    return blocks * marks.astype(jnp.bfloat16)[..., None, None]


def ring_distance(a, b, size):
    d = abs(a - b) % size
    return min(d, size - d)


def to_columns(x, n):
    pairs = []
    for c in range(n):
        targets = sorted(range(n), key=lambda r: (-ring_distance(r, c, n), r))
        sources = sorted(range(n), key=lambda s: (ring_distance(s // 2, c // 2, n // 2), s % 2 != c % 2, s))
        pairs += [(c * n + s, r * n + c) for r, s in zip(targets, sources)]
    return lax.ppermute(x, GRID, pairs)


def tree_sum(parts):
    while len(parts) > 1:
        parts = [parts[i] + parts[i + 1] for i in range(0, len(parts), 2)]
    return parts[0]


def group_sum(x, axis, n, step=1):
    got = [x] + [lax.ppermute(x, axis, [(i, i ^ (step * k)) for i in range(n)]) for k in range(1, n // step)]
    return tree_sum(got)


def column_total(x, n):
    x = x + lax.ppermute(x, "col", [(i, i ^ 1) for i in range(n)])
    return group_sum(x, "col", n, 2)


def products(blocks, segments):
    total = None
    for block, segment in zip(blocks, segments):
        term = jnp.dot(block, segment, preferred_element_type=jnp.float32)
        total = term if total is None else total + term
    return total


def shards(
    rhs,
    rhs_top,
    factor,
    factor_inv,
    lower_bridge,
    upper_bridge,
    top_factor,
    top_inv,
    widths,
    pattern,
    lower_links,
    upper_links,
    top_pattern,
):
    f32 = jnp.float32
    bf16 = jnp.bfloat16
    n = lax.axis_size("row")
    ncol = lax.axis_size("col")
    leaves = lax.axis_size("leaf")
    levels = factor.shape[1]
    tops = top_factor.shape[0]
    block = factor.shape[5]
    sides = rhs.shape[4]
    share = sides // ncol

    fm = masked(factor[0, :, 0, :, 0], pattern[0, :, 0, :, 0])
    lm = masked(lower_bridge[0, :, 0, :, 0], lower_links[0, :, 0, :, 0])
    um = masked(upper_bridge[0, :, 0, :, 0], upper_links[0, :, 0, :, 0])
    tm = masked(top_factor[:, 0, :, 0], top_pattern[:, 0, :, 0])
    marks = lax.broadcasted_iota(jnp.int32, (levels, block, 1), 1)
    keep = (marks < widths[0, :, 0][:, None, None]).astype(f32)
    own_rhs = rhs[0, :, 0]
    inv = factor_inv[0, :, :, 0]
    top_rhs = rhs_top[:, 0]
    tinv = top_inv[:, :, 0]

    ys = []
    segs = []
    for level in range(levels):
        if level == 0:
            resid = own_rhs[0].astype(bf16)
        else:
            part = products([fm[level, j] for j in range(level)], segs)
            resid = (own_rhs[level] - column_total(part, ncol)).astype(bf16)
        solved = keep[level] * jnp.dot(inv[0, level], resid, preferred_element_type=f32)
        ys.append(solved)
        segs.append(to_columns(solved.astype(bf16), n))

    coupling = jnp.stack([products([lm[t, j] for j in range(levels)], segs) for t in range(tops)], 0)
    coupling = group_sum(column_total(coupling, ncol), "leaf", leaves)

    yts = []
    tsegs = []
    for top in range(tops):
        summed = coupling[top]
        if top > 0:
            part = products([tm[top, j] for j in range(top)], tsegs)
            summed = summed + column_total(part, ncol)
        resid = (top_rhs[top] - summed).astype(bf16)
        solved = jnp.dot(tinv[0, top], resid, preferred_element_type=f32)
        yts.append(solved)
        if top < tops - 1:
            tsegs.append(to_columns(solved.astype(bf16), n))

    zts = [None] * tops
    tback = [None] * tops
    for top in reversed(range(tops)):
        if top == tops - 1:
            resid = yts[top].astype(bf16)
        else:
            later = list(reversed(range(top + 1, tops)))
            part = products([tm[top, j] for j in later], [tback[j] for j in later])
            resid = (yts[top] - column_total(part, ncol)).astype(bf16)
        solved = jnp.dot(tinv[1, top], resid, preferred_element_type=f32)
        zts[top] = solved
        tback[top] = to_columns(solved.astype(bf16), n)

    zs = [None] * levels
    back = [None] * levels
    for level in reversed(range(levels)):
        later = list(reversed(range(level + 1, levels)))
        earlier_tops = list(reversed(range(tops)))
        blocks = [um[level, t] for t in earlier_tops] + [fm[level, j] for j in later]
        part = products(blocks, [tback[t] for t in earlier_tops] + [back[j] for j in later])
        resid = (ys[level] - column_total(part, ncol)).astype(bf16)
        solved = keep[level] * jnp.dot(inv[1, level], resid, preferred_element_type=f32)
        zs[level] = solved
        if level > 0:
            back[level] = to_columns(solved.astype(bf16), n)

    start = lax.axis_index("col") * share
    result = lax.dynamic_slice_in_dim(jnp.stack(zs, 0), start, share, 2)
    result_top = lax.dynamic_slice_in_dim(jnp.stack(zts, 0), start, share, 2)
    return (result[None, :, None], result_top[:, None])


def solution(mesh):
    assert mesh.shape["row"] == mesh.shape["col"]
    placed = (
        P("leaf", None, "row", None, None),
        P(None, "row", None, None),
        P("leaf", None, "row", None, "col", None, None),
        P("leaf", None, None, "row", None, None),
        P("leaf", None, "row", None, "col", None, None),
        P("leaf", None, "row", None, "col", None, None),
        P(None, "row", None, "col", None, None),
        P(None, None, "row", None, None),
        P("leaf", None, "row"),
        P("leaf", None, "row", None, "col"),
        P("leaf", None, "row", None, "col"),
        P("leaf", None, "row", None, "col"),
        P(None, "row", None, "col"),
    )
    return jax.shard_map(
        shards,
        mesh=mesh,
        in_specs=placed,
        out_specs=(P("leaf", None, "row", None, "col"), P(None, "row", None, "col")),
        check_vma=False,
    )
```

```python
import jax
import jax.numpy as jnp
from jax import lax
from jax.sharding import PartitionSpec as P

GRID = ("row", "col")


def masked(blocks, marks):
    return blocks * marks.astype(jnp.bfloat16)[..., None, None]


def ring_distance(a, b, size):
    d = abs(a - b) % size
    return min(d, size - d)


def to_columns(x, n):
    pairs = []
    for c in range(n):
        targets = sorted(range(n), key=lambda r: (-ring_distance(r, c, n), r))
        sources = sorted(range(n), key=lambda s: (ring_distance(s // 2, c // 2, n // 2), s % 2 != c % 2, s))
        pairs += [(c * n + s, r * n + c) for r, s in zip(targets, sources)]
    return lax.ppermute(x, GRID, pairs)


def tree_sum(parts):
    while len(parts) > 1:
        parts = [parts[i] + parts[i + 1] for i in range(0, len(parts), 2)]
    return parts[0]


def group_sum(x, axis, n, step=1):
    got = [x] + [lax.ppermute(x, axis, [(i, i ^ (step * k)) for i in range(n)]) for k in range(1, n // step)]
    return tree_sum(got)


def column_total(x, n, leaves=0):
    core = lax.axis_index("col") % 2
    half = x.shape[-1] // 2
    keep_half = lax.dynamic_slice_in_dim(x, core * half, half, x.ndim - 1)
    give_half = lax.dynamic_slice_in_dim(x, (1 - core) * half, half, x.ndim - 1)
    mine = keep_half + lax.ppermute(give_half, "col", [(i, i ^ 1) for i in range(n)])
    mine = group_sum(mine, "col", n, 2)
    if leaves:
        mine = group_sum(mine, "leaf", leaves)
    other = lax.ppermute(mine, "col", [(i, i ^ 1) for i in range(n)])
    first = jnp.where(core == 0, mine, other)
    second = jnp.where(core == 0, other, mine)
    return jnp.concatenate([first, second], x.ndim - 1)


def products(blocks, segments):
    return jnp.einsum(
        "jbk,jkr->br", jnp.stack(blocks, 0), jnp.stack(segments, 0), preferred_element_type=jnp.float32
    )


def shards(
    rhs,
    rhs_top,
    factor,
    factor_inv,
    lower_bridge,
    upper_bridge,
    top_factor,
    top_inv,
    widths,
    pattern,
    lower_links,
    upper_links,
    top_pattern,
):
    f32 = jnp.float32
    bf16 = jnp.bfloat16
    n = lax.axis_size("row")
    ncol = lax.axis_size("col")
    leaves = lax.axis_size("leaf")
    levels = factor.shape[1]
    tops = top_factor.shape[0]
    block = factor.shape[5]
    sides = rhs.shape[4]
    share = sides // ncol

    fm = masked(factor[0, :, 0, :, 0], pattern[0, :, 0, :, 0])
    lm = masked(lower_bridge[0, :, 0, :, 0], lower_links[0, :, 0, :, 0])
    um = masked(upper_bridge[0, :, 0, :, 0], upper_links[0, :, 0, :, 0])
    tm = masked(top_factor[:, 0, :, 0], top_pattern[:, 0, :, 0])
    marks = lax.broadcasted_iota(jnp.int32, (levels, block, 1), 1)
    keep = (marks < widths[0, :, 0][:, None, None]).astype(f32)
    own_rhs = rhs[0, :, 0]
    inv = factor_inv[0, :, :, 0]
    top_rhs = rhs_top[:, 0]
    tinv = top_inv[:, :, 0]

    ys = []
    segs = []
    for level in range(levels):
        if level == 0:
            resid = own_rhs[0].astype(bf16)
        else:
            part = products([fm[level, j] for j in range(level)], segs)
            resid = (own_rhs[level] - column_total(part, ncol)).astype(bf16)
        solved = keep[level] * jnp.dot(inv[0, level], resid, preferred_element_type=f32)
        ys.append(solved)
        segs.append(to_columns(solved.astype(bf16), n))

    coupling = jnp.stack([products([lm[t, j] for j in range(levels)], segs) for t in range(tops)], 0)
    coupling = column_total(coupling, ncol, leaves)

    yts = []
    tsegs = []
    for top in range(tops):
        summed = coupling[top]
        if top > 0:
            part = products([tm[top, j] for j in range(top)], tsegs)
            summed = summed + column_total(part, ncol)
        resid = (top_rhs[top] - summed).astype(bf16)
        solved = jnp.dot(tinv[0, top], resid, preferred_element_type=f32)
        yts.append(solved)
        tsegs.append(to_columns(solved.astype(bf16), n))

    zts = [None] * tops
    tback = [None] * tops
    for top in reversed(range(tops)):
        if top == tops - 1:
            resid = yts[top].astype(bf16)
        else:
            part = products([tm[top, j] for j in range(top + 1, tops)], tback[top + 1 :])
            resid = (yts[top] - column_total(part, ncol)).astype(bf16)
        solved = jnp.dot(tinv[1, top], resid, preferred_element_type=f32)
        zts[top] = solved
        tback[top] = to_columns(solved.astype(bf16), n)

    zs = [None] * levels
    back = [None] * levels
    for level in reversed(range(levels)):
        blocks = [um[level, t] for t in range(tops)] + [fm[level, j] for j in range(level + 1, levels)]
        part = products(blocks, tback + back[level + 1 :])
        resid = (ys[level] - column_total(part, ncol)).astype(bf16)
        solved = keep[level] * jnp.dot(inv[1, level], resid, preferred_element_type=f32)
        zs[level] = solved
        if level > 0:
            back[level] = to_columns(solved.astype(bf16), n)

    start = lax.axis_index("col") * share
    result = lax.dynamic_slice_in_dim(jnp.stack(zs, 0), start, share, 2)
    result_top = lax.dynamic_slice_in_dim(jnp.stack(zts, 0), start, share, 2)
    return (result[None, :, None], result_top[:, None])


def solution(mesh):
    assert mesh.shape["row"] == mesh.shape["col"]
    placed = (
        P("leaf", None, "row", None, None),
        P(None, "row", None, None),
        P("leaf", None, "row", None, "col", None, None),
        P("leaf", None, None, "row", None, None),
        P("leaf", None, "row", None, "col", None, None),
        P("leaf", None, "row", None, "col", None, None),
        P(None, "row", None, "col", None, None),
        P(None, None, "row", None, None),
        P("leaf", None, "row"),
        P("leaf", None, "row", None, "col"),
        P("leaf", None, "row", None, "col"),
        P("leaf", None, "row", None, "col"),
        P(None, "row", None, "col"),
    )
    return jax.shard_map(
        shards,
        mesh=mesh,
        in_specs=placed,
        out_specs=(P("leaf", None, "row", None, "col"), P(None, "row", None, "col")),
        check_vma=False,
    )
```

```python
import jax
import jax.numpy as jnp
from jax import lax
from jax.sharding import PartitionSpec as P

GRID = ("row", "col")


def masked(blocks, marks):
    return blocks * marks.astype(jnp.bfloat16)[..., None, None]


def ring_distance(a, b, size):
    d = abs(a - b) % size
    return min(d, size - d)


def to_columns(x, n):
    pairs = []
    for c in range(n):
        targets = sorted(range(n), key=lambda r: (-ring_distance(r, c, n), r))
        sources = sorted(range(n), key=lambda s: (ring_distance(s // 2, c // 2, n // 2), s % 2 != c % 2, s))
        pairs += [(c * n + s, r * n + c) for r, s in zip(targets, sources)]
    return lax.ppermute(x, GRID, pairs)


def tree_sum(parts):
    while len(parts) > 1:
        parts = [parts[i] + parts[i + 1] for i in range(0, len(parts), 2)]
    return parts[0]


def group_sum(x, axis, n, step=1):
    got = [x] + [lax.ppermute(x, axis, [(i, i ^ (step * k)) for i in range(n)]) for k in range(1, n // step)]
    return tree_sum(got)


def column_total(x, n, leaves=0):
    core = lax.axis_index("col") % 2
    half = x.shape[-1] // 2
    keep_half = lax.dynamic_slice_in_dim(x, core * half, half, x.ndim - 1)
    give_half = lax.dynamic_slice_in_dim(x, (1 - core) * half, half, x.ndim - 1)
    mine = keep_half + lax.ppermute(give_half, "col", [(i, i ^ 1) for i in range(n)])
    mine = group_sum(mine, "col", n, 2)
    if leaves:
        mine = group_sum(mine, "leaf", leaves)
    return mine


def join_halves(mine, n):
    core = lax.axis_index("col") % 2
    other = lax.ppermute(mine, "col", [(i, i ^ 1) for i in range(n)])
    first = jnp.where(core == 0, mine, other)
    second = jnp.where(core == 0, other, mine)
    return jnp.concatenate([first, second], mine.ndim - 1)


def own_half(x, ncol):
    chunk = x.shape[-1] // ncol
    lead = x.shape[:-1]
    x = x.reshape(lead + (ncol // 2, 2, chunk))
    x = jnp.moveaxis(x, -2, -3).reshape(lead + (x.shape[-1] * ncol,))
    half = x.shape[-1] // 2
    return lax.dynamic_slice_in_dim(x, (lax.axis_index("col") % 2) * half, half, x.ndim - 1)


def products(blocks, segments):
    return jnp.einsum(
        "jbk,jkr->br", jnp.stack(blocks, 0), jnp.stack(segments, 0), preferred_element_type=jnp.float32
    )


def shards(
    rhs,
    rhs_top,
    factor,
    factor_inv,
    lower_bridge,
    upper_bridge,
    top_factor,
    top_inv,
    widths,
    pattern,
    lower_links,
    upper_links,
    top_pattern,
):
    f32 = jnp.float32
    bf16 = jnp.bfloat16
    n = lax.axis_size("row")
    ncol = lax.axis_size("col")
    leaves = lax.axis_size("leaf")
    levels = factor.shape[1]
    tops = top_factor.shape[0]
    block = factor.shape[5]
    sides = rhs.shape[4]
    share = sides // ncol

    fm = masked(factor[0, :, 0, :, 0], pattern[0, :, 0, :, 0])
    lm = masked(lower_bridge[0, :, 0, :, 0], lower_links[0, :, 0, :, 0])
    um = masked(upper_bridge[0, :, 0, :, 0], upper_links[0, :, 0, :, 0])
    tm = masked(top_factor[:, 0, :, 0], top_pattern[:, 0, :, 0])
    marks = lax.broadcasted_iota(jnp.int32, (levels, block, 1), 1)
    keep = (marks < widths[0, :, 0][:, None, None]).astype(f32)
    own_rhs = own_half(rhs[0, :, 0], ncol)
    inv = factor_inv[0, :, :, 0]
    top_rhs = own_half(rhs_top[:, 0], ncol)
    tinv = top_inv[:, :, 0]

    ys = []
    segs = []
    for level in range(levels):
        if level == 0:
            resid = own_rhs[0].astype(bf16)
        else:
            part = products([fm[level, j] for j in range(level)], segs)
            resid = (own_rhs[level] - column_total(part, ncol)).astype(bf16)
        solved = keep[level] * jnp.dot(inv[0, level], resid, preferred_element_type=f32)
        ys.append(solved)
        segs.append(to_columns(join_halves(solved.astype(bf16), ncol), n))

    coupling = jnp.stack([products([lm[t, j] for j in range(levels)], segs) for t in range(tops)], 0)
    coupling = column_total(coupling, ncol, leaves)

    yts = []
    tsegs = []
    for top in range(tops):
        summed = coupling[top]
        if top > 0:
            part = products([tm[top, j] for j in range(top)], tsegs)
            summed = summed + column_total(part, ncol)
        resid = (top_rhs[top] - summed).astype(bf16)
        solved = jnp.dot(tinv[0, top], resid, preferred_element_type=f32)
        yts.append(solved)
        tsegs.append(to_columns(join_halves(solved.astype(bf16), ncol), n))

    zts = [None] * tops
    tback = [None] * tops
    for top in reversed(range(tops)):
        if top == tops - 1:
            resid = yts[top].astype(bf16)
        else:
            part = products([tm[top, j] for j in range(top + 1, tops)], tback[top + 1 :])
            resid = (yts[top] - column_total(part, ncol)).astype(bf16)
        solved = jnp.dot(tinv[1, top], resid, preferred_element_type=f32)
        zts[top] = solved
        tback[top] = to_columns(join_halves(solved.astype(bf16), ncol), n)

    zs = [None] * levels
    back = [None] * levels
    for level in reversed(range(levels)):
        blocks = [um[level, t] for t in range(tops)] + [fm[level, j] for j in range(level + 1, levels)]
        part = products(blocks, tback + back[level + 1 :])
        resid = (ys[level] - column_total(part, ncol)).astype(bf16)
        solved = keep[level] * jnp.dot(inv[1, level], resid, preferred_element_type=f32)
        zs[level] = solved
        if level > 0:
            back[level] = to_columns(join_halves(solved.astype(bf16), ncol), n)

    start = (lax.axis_index("col") // 2) * share
    result = lax.dynamic_slice_in_dim(jnp.stack(zs, 0), start, share, 2)
    result_top = lax.dynamic_slice_in_dim(jnp.stack(zts, 0), start, share, 2)
    return (result[None, :, None], result_top[:, None])


def solution(mesh):
    assert mesh.shape["row"] == mesh.shape["col"]
    placed = (
        P("leaf", None, "row", None, None),
        P(None, "row", None, None),
        P("leaf", None, "row", None, "col", None, None),
        P("leaf", None, None, "row", None, None),
        P("leaf", None, "row", None, "col", None, None),
        P("leaf", None, "row", None, "col", None, None),
        P(None, "row", None, "col", None, None),
        P(None, None, "row", None, None),
        P("leaf", None, "row"),
        P("leaf", None, "row", None, "col"),
        P("leaf", None, "row", None, "col"),
        P("leaf", None, "row", None, "col"),
        P(None, "row", None, "col"),
    )
    return jax.shard_map(
        shards,
        mesh=mesh,
        in_specs=placed,
        out_specs=(P("leaf", None, "row", None, "col"), P(None, "row", None, "col")),
        check_vma=False,
    )
```

```python
import jax
import jax.numpy as jnp
from jax import lax
from jax.sharding import PartitionSpec as P

GRID = ("row", "col")


def masked(blocks, marks):
    return blocks * marks.astype(jnp.bfloat16)[..., None, None]


def ring_distance(a, b, size):
    d = abs(a - b) % size
    return min(d, size - d)


def to_columns(x, n):
    pairs = []
    for c in range(n):
        targets = sorted(range(n), key=lambda r: (-ring_distance(r, c, n), r))
        sources = sorted(range(n), key=lambda s: (ring_distance(s // 2, c // 2, n // 2), s % 2 != c % 2, s))
        pairs += [(c * n + s, r * n + c) for r, s in zip(targets, sources)]
    return lax.ppermute(x, GRID, pairs)


def halves_to_columns(mine, n):
    r_me = lax.axis_index("row")
    c_me = lax.axis_index("col")
    got = []
    for h in range(2):
        first = [[False] * n for _ in range(n)]
        rounds = [[], []]
        for c in range(n):
            targets = sorted(range(n), key=lambda r: (-ring_distance(r, c, n), r))
            sources = sorted(range(h, n, 2), key=lambda s: (ring_distance(s // 2, c // 2, n // 2), s))
            for i, r in enumerate(targets):
                rounds[i // len(sources)].append((c * n + sources[i % len(sources)], r * n + c))
                first[r][c] = i < len(sources)
        sent = [lax.ppermute(mine, GRID, pairs) for pairs in rounds]
        pick = jnp.asarray(first)[r_me, c_me]
        got.append(jnp.where(pick, sent[0], sent[1]))
    return jnp.concatenate(got, mine.ndim - 1)


def tree_sum(parts):
    while len(parts) > 1:
        parts = [parts[i] + parts[i + 1] for i in range(0, len(parts), 2)]
    return parts[0]


def group_sum(x, axis, n, step=1):
    got = [x] + [lax.ppermute(x, axis, [(i, i ^ (step * k)) for i in range(n)]) for k in range(1, n // step)]
    return tree_sum(got)


def column_total(x, n, leaves=0):
    core = lax.axis_index("col") % 2
    half = x.shape[-1] // 2
    keep_half = lax.dynamic_slice_in_dim(x, core * half, half, x.ndim - 1)
    give_half = lax.dynamic_slice_in_dim(x, (1 - core) * half, half, x.ndim - 1)
    mine = keep_half + lax.ppermute(give_half, "col", [(i, i ^ 1) for i in range(n)])
    mine = group_sum(mine, "col", n, 2)
    if leaves:
        mine = group_sum(mine, "leaf", leaves)
    return mine


def join_halves(mine, n):
    core = lax.axis_index("col") % 2
    other = lax.ppermute(mine, "col", [(i, i ^ 1) for i in range(n)])
    first = jnp.where(core == 0, mine, other)
    second = jnp.where(core == 0, other, mine)
    return jnp.concatenate([first, second], mine.ndim - 1)


def own_half(x, ncol):
    chunk = x.shape[-1] // ncol
    lead = x.shape[:-1]
    x = x.reshape(lead + (ncol // 2, 2, chunk))
    x = jnp.moveaxis(x, -2, -3).reshape(lead + (x.shape[-1] * ncol,))
    half = x.shape[-1] // 2
    return lax.dynamic_slice_in_dim(x, (lax.axis_index("col") % 2) * half, half, x.ndim - 1)


def products(blocks, segments):
    return jnp.einsum(
        "jbk,jkr->br", jnp.stack(blocks, 0), jnp.stack(segments, 0), preferred_element_type=jnp.float32
    )


def shards(
    rhs,
    rhs_top,
    factor,
    factor_inv,
    lower_bridge,
    upper_bridge,
    top_factor,
    top_inv,
    widths,
    pattern,
    lower_links,
    upper_links,
    top_pattern,
):
    f32 = jnp.float32
    bf16 = jnp.bfloat16
    n = lax.axis_size("row")
    ncol = lax.axis_size("col")
    leaves = lax.axis_size("leaf")
    levels = factor.shape[1]
    tops = top_factor.shape[0]
    block = factor.shape[5]
    sides = rhs.shape[4]
    share = sides // ncol

    fm = masked(factor[0, :, 0, :, 0], pattern[0, :, 0, :, 0])
    lm = masked(lower_bridge[0, :, 0, :, 0], lower_links[0, :, 0, :, 0])
    um = masked(upper_bridge[0, :, 0, :, 0], upper_links[0, :, 0, :, 0])
    tm = masked(top_factor[:, 0, :, 0], top_pattern[:, 0, :, 0])
    marks = lax.broadcasted_iota(jnp.int32, (levels, block, 1), 1)
    keep = (marks < widths[0, :, 0][:, None, None]).astype(f32)
    own_rhs = own_half(rhs[0, :, 0], ncol)
    inv = factor_inv[0, :, :, 0]
    top_rhs = own_half(rhs_top[:, 0], ncol)
    tinv = top_inv[:, :, 0]

    ys = []
    segs = []
    for level in range(levels):
        if level == 0:
            resid = own_rhs[0].astype(bf16)
        else:
            part = products([fm[level, j] for j in range(level)], segs)
            resid = (own_rhs[level] - column_total(part, ncol)).astype(bf16)
        solved = keep[level] * jnp.dot(inv[0, level], resid, preferred_element_type=f32)
        ys.append(solved)
        segs.append(halves_to_columns(solved.astype(bf16), n))

    coupling = jnp.stack([products([lm[t, j] for j in range(levels)], segs) for t in range(tops)], 0)
    coupling = column_total(coupling, ncol, leaves)

    yts = []
    tsegs = []
    for top in range(tops):
        summed = coupling[top]
        if top > 0:
            part = products([tm[top, j] for j in range(top)], tsegs)
            summed = summed + column_total(part, ncol)
        resid = (top_rhs[top] - summed).astype(bf16)
        solved = jnp.dot(tinv[0, top], resid, preferred_element_type=f32)
        yts.append(solved)
        tsegs.append(halves_to_columns(solved.astype(bf16), n))

    zts = [None] * tops
    tback = [None] * tops
    for top in reversed(range(tops)):
        if top == tops - 1:
            resid = yts[top].astype(bf16)
        else:
            part = products([tm[top, j] for j in range(top + 1, tops)], tback[top + 1 :])
            resid = (yts[top] - column_total(part, ncol)).astype(bf16)
        solved = jnp.dot(tinv[1, top], resid, preferred_element_type=f32)
        zts[top] = solved
        tback[top] = halves_to_columns(solved.astype(bf16), n)

    zs = [None] * levels
    back = [None] * levels
    for level in reversed(range(levels)):
        blocks = [um[level, t] for t in range(tops)] + [fm[level, j] for j in range(level + 1, levels)]
        part = products(blocks, tback + back[level + 1 :])
        resid = (ys[level] - column_total(part, ncol)).astype(bf16)
        solved = keep[level] * jnp.dot(inv[1, level], resid, preferred_element_type=f32)
        zs[level] = solved
        if level > 0:
            back[level] = halves_to_columns(solved.astype(bf16), n)

    start = (lax.axis_index("col") // 2) * share
    result = lax.dynamic_slice_in_dim(jnp.stack(zs, 0), start, share, 2)
    result_top = lax.dynamic_slice_in_dim(jnp.stack(zts, 0), start, share, 2)
    return (result[None, :, None], result_top[:, None])


def solution(mesh):
    assert mesh.shape["row"] == mesh.shape["col"]
    placed = (
        P("leaf", None, "row", None, None),
        P(None, "row", None, None),
        P("leaf", None, "row", None, "col", None, None),
        P("leaf", None, None, "row", None, None),
        P("leaf", None, "row", None, "col", None, None),
        P("leaf", None, "row", None, "col", None, None),
        P(None, "row", None, "col", None, None),
        P(None, None, "row", None, None),
        P("leaf", None, "row"),
        P("leaf", None, "row", None, "col"),
        P("leaf", None, "row", None, "col"),
        P("leaf", None, "row", None, "col"),
        P(None, "row", None, "col"),
    )
    return jax.shard_map(
        shards,
        mesh=mesh,
        in_specs=placed,
        out_specs=(P("leaf", None, "row", None, "col"), P(None, "row", None, "col")),
        check_vma=False,
    )
```

```python
import jax
import jax.numpy as jnp
from jax import lax
from jax.sharding import PartitionSpec as P

GRID = ("row", "col")


def masked(blocks, marks):
    return blocks * marks.astype(jnp.bfloat16)[..., None, None]


def ring_distance(a, b, size):
    d = abs(a - b) % size
    return min(d, size - d)


def to_columns(x, n):
    pairs = []
    for c in range(n):
        targets = sorted(range(n), key=lambda r: (-ring_distance(r, c, n), r))
        sources = sorted(range(n), key=lambda s: (ring_distance(s // 2, c // 2, n // 2), s % 2 != c % 2, s))
        pairs += [(c * n + s, r * n + c) for r, s in zip(targets, sources)]
    return lax.ppermute(x, GRID, pairs)


def tree_sum(parts):
    while len(parts) > 1:
        parts = [parts[i] + parts[i + 1] for i in range(0, len(parts), 2)]
    return parts[0]


def group_sum(x, axis, n, step=1):
    got = [x] + [lax.ppermute(x, axis, [(i, i ^ (step * k)) for i in range(n)]) for k in range(1, n // step)]
    return tree_sum(got)


def column_total(x, n, leaves=0):
    core = lax.axis_index("col") % 2
    half = x.shape[-1] // 2
    keep_half = lax.dynamic_slice_in_dim(x, core * half, half, x.ndim - 1)
    give_half = lax.dynamic_slice_in_dim(x, (1 - core) * half, half, x.ndim - 1)
    mine = keep_half + lax.ppermute(give_half, "col", [(i, i ^ 1) for i in range(n)])
    mine = group_sum(mine, "col", n, 2)
    if leaves:
        mine = group_sum(mine, "leaf", leaves)
    return mine


def join_halves(mine, n):
    core = lax.axis_index("col") % 2
    other = lax.ppermute(mine, "col", [(i, i ^ 1) for i in range(n)])
    first = jnp.where(core == 0, mine, other)
    second = jnp.where(core == 0, other, mine)
    return jnp.concatenate([first, second], mine.ndim - 1)


def own_half(x, ncol):
    chunk = x.shape[-1] // ncol
    lead = x.shape[:-1]
    x = x.reshape(lead + (ncol // 2, 2, chunk))
    x = jnp.moveaxis(x, -2, -3).reshape(lead + (x.shape[-1] * ncol,))
    half = x.shape[-1] // 2
    return lax.dynamic_slice_in_dim(x, (lax.axis_index("col") % 2) * half, half, x.ndim - 1)


def products(blocks, segments):
    return jnp.einsum(
        "jbk,jkr->br", jnp.stack(blocks, 0), jnp.stack(segments, 0), preferred_element_type=jnp.float32
    )


def shards(
    rhs,
    rhs_top,
    factor,
    factor_inv,
    lower_bridge,
    upper_bridge,
    top_factor,
    top_inv,
    widths,
    pattern,
    lower_links,
    upper_links,
    top_pattern,
):
    f32 = jnp.float32
    bf16 = jnp.bfloat16
    n = lax.axis_size("row")
    ncol = lax.axis_size("col")
    leaves = lax.axis_size("leaf")
    levels = factor.shape[1]
    tops = top_factor.shape[0]
    block = factor.shape[5]
    sides = rhs.shape[4]
    share = sides // ncol

    fm = masked(factor[0, :, 0, :, 0], pattern[0, :, 0, :, 0])
    lm = masked(lower_bridge[0, :, 0, :, 0], lower_links[0, :, 0, :, 0])
    um = masked(upper_bridge[0, :, 0, :, 0], upper_links[0, :, 0, :, 0])
    tm = masked(top_factor[:, 0, :, 0], top_pattern[:, 0, :, 0])
    marks = lax.broadcasted_iota(jnp.int32, (levels, block, 1), 1)
    keep = (marks < widths[0, :, 0][:, None, None]).astype(f32)
    own_rhs = own_half(rhs[0, :, 0], ncol)
    inv = factor_inv[0, :, :, 0]
    top_rhs = own_half(rhs_top[:, 0], ncol)
    tinv = top_inv[:, :, 0]

    ys = []
    segs = []
    for level in range(levels):
        if level == 0:
            resid = own_rhs[0].astype(bf16)
        else:
            part = products([fm[level, j] for j in range(level)], segs)
            resid = (own_rhs[level] - column_total(part, ncol)).astype(bf16)
        solved = keep[level] * jnp.dot(inv[0, level], resid, preferred_element_type=f32)
        ys.append(solved)
        segs.append(to_columns(join_halves(solved.astype(bf16), ncol), n))

    coupling = [column_total(products([lm[t, j] for j in range(levels)], segs), ncol, leaves) for t in range(tops)]

    yts = []
    tsegs = []
    for top in range(tops):
        summed = coupling[top]
        if top > 0:
            part = products([tm[top, j] for j in range(top)], tsegs)
            summed = summed + column_total(part, ncol)
        resid = (top_rhs[top] - summed).astype(bf16)
        solved = jnp.dot(tinv[0, top], resid, preferred_element_type=f32)
        yts.append(solved)
        tsegs.append(to_columns(join_halves(solved.astype(bf16), ncol), n))

    zts = [None] * tops
    tback = [None] * tops
    for top in reversed(range(tops)):
        if top == tops - 1:
            resid = yts[top].astype(bf16)
        else:
            part = products([tm[top, j] for j in range(top + 1, tops)], tback[top + 1 :])
            resid = (yts[top] - column_total(part, ncol)).astype(bf16)
        solved = jnp.dot(tinv[1, top], resid, preferred_element_type=f32)
        zts[top] = solved
        tback[top] = to_columns(join_halves(solved.astype(bf16), ncol), n)

    zs = [None] * levels
    back = [None] * levels
    for level in reversed(range(levels)):
        blocks = [um[level, t] for t in range(tops)] + [fm[level, j] for j in range(level + 1, levels)]
        part = products(blocks, tback + back[level + 1 :])
        resid = (ys[level] - column_total(part, ncol)).astype(bf16)
        solved = keep[level] * jnp.dot(inv[1, level], resid, preferred_element_type=f32)
        zs[level] = solved
        if level > 0:
            back[level] = to_columns(join_halves(solved.astype(bf16), ncol), n)

    start = (lax.axis_index("col") // 2) * share
    result = lax.dynamic_slice_in_dim(jnp.stack(zs, 0), start, share, 2)
    result_top = lax.dynamic_slice_in_dim(jnp.stack(zts, 0), start, share, 2)
    return (result[None, :, None], result_top[:, None])


def solution(mesh):
    assert mesh.shape["row"] == mesh.shape["col"]
    placed = (
        P("leaf", None, "row", None, None),
        P(None, "row", None, None),
        P("leaf", None, "row", None, "col", None, None),
        P("leaf", None, None, "row", None, None),
        P("leaf", None, "row", None, "col", None, None),
        P("leaf", None, "row", None, "col", None, None),
        P(None, "row", None, "col", None, None),
        P(None, None, "row", None, None),
        P("leaf", None, "row"),
        P("leaf", None, "row", None, "col"),
        P("leaf", None, "row", None, "col"),
        P("leaf", None, "row", None, "col"),
        P(None, "row", None, "col"),
    )
    return jax.shard_map(
        shards,
        mesh=mesh,
        in_specs=placed,
        out_specs=(P("leaf", None, "row", None, "col"), P(None, "row", None, "col")),
        check_vma=False,
    )
```

```python
import jax
import jax.numpy as jnp
from jax import lax
from jax.sharding import PartitionSpec as P

GRID = ("row", "col")


def masked(blocks, marks):
    return blocks * marks.astype(jnp.bfloat16)[..., None, None]


def ring_distance(a, b, size):
    d = abs(a - b) % size
    return min(d, size - d)


def to_columns(x, n):
    pairs = []
    for c in range(n):
        targets = sorted(range(n), key=lambda r: (-ring_distance(r, c, n), r))
        sources = sorted(range(n), key=lambda s: (ring_distance(s // 2, c // 2, n // 2), s % 2 != c % 2, s))
        pairs += [(c * n + s, r * n + c) for r, s in zip(targets, sources)]
    return lax.ppermute(x, GRID, pairs)


def tree_sum(parts):
    while len(parts) > 1:
        parts = [parts[i] + parts[i + 1] for i in range(0, len(parts), 2)]
    return parts[0]


def group_sum(x, axis, n, step=1):
    got = [x] + [lax.ppermute(x, axis, [(i, i ^ (step * k)) for i in range(n)]) for k in range(1, n // step)]
    return tree_sum(got)


def column_total(x, n, leaves=0):
    core = lax.axis_index("col") % 2
    half = x.shape[-1] // 2
    keep_half = lax.dynamic_slice_in_dim(x, core * half, half, x.ndim - 1)
    give_half = lax.dynamic_slice_in_dim(x, (1 - core) * half, half, x.ndim - 1)
    mine = keep_half + lax.ppermute(give_half, "col", [(i, i ^ 1) for i in range(n)])
    mine = group_sum(mine, "col", n, 2)
    if leaves:
        mine = group_sum(mine, "leaf", leaves)
    return mine


def column_chunk_total(x, n):
    core = lax.axis_index("col") % 2
    chip = lax.axis_index("col") // 2
    half = x.shape[-1] // 2
    keep_half = lax.dynamic_slice_in_dim(x, core * half, half, x.ndim - 1)
    give_half = lax.dynamic_slice_in_dim(x, (1 - core) * half, half, x.ndim - 1)
    mine = keep_half + lax.ppermute(give_half, "col", [(i, i ^ 1) for i in range(n)])
    chips = n // 2
    chunk = half // chips
    got = [lax.dynamic_slice_in_dim(mine, chip * chunk, chunk, x.ndim - 1)]
    for k in range(1, chips):
        piece = lax.dynamic_slice_in_dim(mine, (chip ^ k) * chunk, chunk, x.ndim - 1)
        got.append(lax.ppermute(piece, "col", [(i, i ^ (2 * k)) for i in range(n)]))
    return tree_sum(got)


def join_halves(mine, n):
    core = lax.axis_index("col") % 2
    other = lax.ppermute(mine, "col", [(i, i ^ 1) for i in range(n)])
    first = jnp.where(core == 0, mine, other)
    second = jnp.where(core == 0, other, mine)
    return jnp.concatenate([first, second], mine.ndim - 1)


def own_half(x, ncol):
    chunk = x.shape[-1] // ncol
    lead = x.shape[:-1]
    x = x.reshape(lead + (ncol // 2, 2, chunk))
    x = jnp.moveaxis(x, -2, -3).reshape(lead + (x.shape[-1] * ncol,))
    half = x.shape[-1] // 2
    return lax.dynamic_slice_in_dim(x, (lax.axis_index("col") % 2) * half, half, x.ndim - 1)


def products(blocks, segments):
    return jnp.einsum(
        "jbk,jkr->br", jnp.stack(blocks, 0), jnp.stack(segments, 0), preferred_element_type=jnp.float32
    )


def shards(
    rhs,
    rhs_top,
    factor,
    factor_inv,
    lower_bridge,
    upper_bridge,
    top_factor,
    top_inv,
    widths,
    pattern,
    lower_links,
    upper_links,
    top_pattern,
):
    f32 = jnp.float32
    bf16 = jnp.bfloat16
    n = lax.axis_size("row")
    ncol = lax.axis_size("col")
    leaves = lax.axis_size("leaf")
    levels = factor.shape[1]
    tops = top_factor.shape[0]
    block = factor.shape[5]
    sides = rhs.shape[4]
    share = sides // ncol

    fm = masked(factor[0, :, 0, :, 0], pattern[0, :, 0, :, 0])
    lm = masked(lower_bridge[0, :, 0, :, 0], lower_links[0, :, 0, :, 0])
    um = masked(upper_bridge[0, :, 0, :, 0], upper_links[0, :, 0, :, 0])
    tm = masked(top_factor[:, 0, :, 0], top_pattern[:, 0, :, 0])
    marks = lax.broadcasted_iota(jnp.int32, (levels, block, 1), 1)
    keep = (marks < widths[0, :, 0][:, None, None]).astype(f32)
    own_rhs = own_half(rhs[0, :, 0], ncol)
    inv = factor_inv[0, :, :, 0]
    top_rhs = own_half(rhs_top[:, 0], ncol)
    tinv = top_inv[:, :, 0]

    ys = []
    segs = []
    for level in range(levels):
        if level == 0:
            resid = own_rhs[0].astype(bf16)
        else:
            part = products([fm[level, j] for j in range(level)], segs)
            resid = (own_rhs[level] - column_total(part, ncol)).astype(bf16)
        solved = keep[level] * jnp.dot(inv[0, level], resid, preferred_element_type=f32)
        ys.append(solved)
        segs.append(to_columns(join_halves(solved.astype(bf16), ncol), n))

    coupling = [column_total(products([lm[t, j] for j in range(levels)], segs), ncol, leaves) for t in range(tops)]

    yts = []
    tsegs = []
    for top in range(tops):
        summed = coupling[top]
        if top > 0:
            part = products([tm[top, j] for j in range(top)], tsegs)
            summed = summed + column_total(part, ncol)
        resid = (top_rhs[top] - summed).astype(bf16)
        solved = jnp.dot(tinv[0, top], resid, preferred_element_type=f32)
        yts.append(solved)
        tsegs.append(to_columns(join_halves(solved.astype(bf16), ncol), n))

    zts = [None] * tops
    tback = [None] * tops
    for top in reversed(range(tops)):
        if top == tops - 1:
            resid = yts[top].astype(bf16)
        else:
            part = products([tm[top, j] for j in range(top + 1, tops)], tback[top + 1 :])
            resid = (yts[top] - column_total(part, ncol)).astype(bf16)
        solved = jnp.dot(tinv[1, top], resid, preferred_element_type=f32)
        zts[top] = solved
        tback[top] = to_columns(join_halves(solved.astype(bf16), ncol), n)

    zs = [None] * levels
    back = [None] * levels
    for level in reversed(range(levels)):
        blocks = [um[level, t] for t in range(tops)] + [fm[level, j] for j in range(level + 1, levels)]
        part = products(blocks, tback + back[level + 1 :])
        if level > 0:
            resid = (ys[level] - column_total(part, ncol)).astype(bf16)
        else:
            mine = lax.dynamic_slice_in_dim(ys[level], (lax.axis_index("col") // 2) * share, share, 1)
            resid = (mine - column_chunk_total(part, ncol)).astype(bf16)
        solved = keep[level] * jnp.dot(inv[1, level], resid, preferred_element_type=f32)
        zs[level] = solved
        if level > 0:
            back[level] = to_columns(join_halves(solved.astype(bf16), ncol), n)

    start = (lax.axis_index("col") // 2) * share
    result = jnp.stack([zs[0]] + [lax.dynamic_slice_in_dim(z, start, share, 1) for z in zs[1:]], 0)
    result_top = lax.dynamic_slice_in_dim(jnp.stack(zts, 0), start, share, 2)
    return (result[None, :, None], result_top[:, None])


def solution(mesh):
    assert mesh.shape["row"] == mesh.shape["col"]
    placed = (
        P("leaf", None, "row", None, None),
        P(None, "row", None, None),
        P("leaf", None, "row", None, "col", None, None),
        P("leaf", None, None, "row", None, None),
        P("leaf", None, "row", None, "col", None, None),
        P("leaf", None, "row", None, "col", None, None),
        P(None, "row", None, "col", None, None),
        P(None, None, "row", None, None),
        P("leaf", None, "row"),
        P("leaf", None, "row", None, "col"),
        P("leaf", None, "row", None, "col"),
        P("leaf", None, "row", None, "col"),
        P(None, "row", None, "col"),
    )
    return jax.shard_map(
        shards,
        mesh=mesh,
        in_specs=placed,
        out_specs=(P("leaf", None, "row", None, "col"), P(None, "row", None, "col")),
        check_vma=False,
    )
```

```python
import jax
import jax.numpy as jnp
from jax import lax
from jax.sharding import PartitionSpec as P

GRID = ("row", "col")


def masked(blocks, marks):
    return blocks * marks.astype(jnp.bfloat16)[..., None, None]


def ring_distance(a, b, size):
    d = abs(a - b) % size
    return min(d, size - d)


def to_columns(x, n):
    pairs = []
    for c in range(n):
        targets = sorted(range(n), key=lambda r: (-ring_distance(r, c, n), r))
        sources = sorted(range(n), key=lambda s: (ring_distance(s // 2, c // 2, n // 2), s % 2 != c % 2, s))
        pairs += [(c * n + s, r * n + c) for r, s in zip(targets, sources)]
    return lax.ppermute(x, GRID, pairs)


def tree_sum(parts):
    while len(parts) > 1:
        parts = [parts[i] + parts[i + 1] for i in range(0, len(parts), 2)]
    return parts[0]


def group_sum(x, axis, n, step=1):
    got = [x] + [lax.ppermute(x, axis, [(i, i ^ (step * k)) for i in range(n)]) for k in range(1, n // step)]
    return tree_sum(got)


def column_total(x, n, leaves=0):
    core = lax.axis_index("col") % 2
    half = x.shape[-1] // 2
    keep_half = lax.dynamic_slice_in_dim(x, core * half, half, x.ndim - 1)
    give_half = lax.dynamic_slice_in_dim(x, (1 - core) * half, half, x.ndim - 1)
    mine = keep_half + lax.ppermute(give_half, "col", [(i, i ^ 1) for i in range(n)])
    mine = group_sum(mine, "col", n, 2)
    if leaves:
        mine = group_sum(mine, "leaf", leaves)
    return mine


def column_chunk_total(x, n, leaves=0):
    core = lax.axis_index("col") % 2
    chip = lax.axis_index("col") // 2
    half = x.shape[-1] // 2
    keep_half = lax.dynamic_slice_in_dim(x, core * half, half, x.ndim - 1)
    give_half = lax.dynamic_slice_in_dim(x, (1 - core) * half, half, x.ndim - 1)
    mine = keep_half + lax.ppermute(give_half, "col", [(i, i ^ 1) for i in range(n)])
    chips = n // 2
    chunk = half // chips
    got = [lax.dynamic_slice_in_dim(mine, chip * chunk, chunk, x.ndim - 1)]
    for k in range(1, chips):
        piece = lax.dynamic_slice_in_dim(mine, (chip ^ k) * chunk, chunk, x.ndim - 1)
        got.append(lax.ppermute(piece, "col", [(i, i ^ (2 * k)) for i in range(n)]))
    total = tree_sum(got)
    if leaves:
        total = group_sum(total, "leaf", leaves)
    return total


def join_chunks(mine, n):
    chips = n // 2
    chip = lax.axis_index("col") // 2
    got = jnp.stack([mine] + [lax.ppermute(mine, "col", [(i, i ^ (2 * k)) for i in range(n)]) for k in range(1, chips)], 0)
    got = jnp.take(got, chip ^ jnp.arange(chips), axis=0)
    half = jnp.moveaxis(got, 0, -2).reshape(mine.shape[:-1] + (chips * mine.shape[-1],))
    return join_halves(half, n)


def join_halves(mine, n):
    core = lax.axis_index("col") % 2
    other = lax.ppermute(mine, "col", [(i, i ^ 1) for i in range(n)])
    first = jnp.where(core == 0, mine, other)
    second = jnp.where(core == 0, other, mine)
    return jnp.concatenate([first, second], mine.ndim - 1)


def own_half(x, ncol):
    chunk = x.shape[-1] // ncol
    lead = x.shape[:-1]
    x = x.reshape(lead + (ncol // 2, 2, chunk))
    x = jnp.moveaxis(x, -2, -3).reshape(lead + (x.shape[-1] * ncol,))
    half = x.shape[-1] // 2
    return lax.dynamic_slice_in_dim(x, (lax.axis_index("col") % 2) * half, half, x.ndim - 1)


def products(blocks, segments):
    return jnp.einsum(
        "jbk,jkr->br", jnp.stack(blocks, 0), jnp.stack(segments, 0), preferred_element_type=jnp.float32
    )


def shards(
    rhs,
    rhs_top,
    factor,
    factor_inv,
    lower_bridge,
    upper_bridge,
    top_factor,
    top_inv,
    widths,
    pattern,
    lower_links,
    upper_links,
    top_pattern,
):
    f32 = jnp.float32
    bf16 = jnp.bfloat16
    n = lax.axis_size("row")
    ncol = lax.axis_size("col")
    leaves = lax.axis_size("leaf")
    levels = factor.shape[1]
    tops = top_factor.shape[0]
    block = factor.shape[5]
    sides = rhs.shape[4]
    share = sides // ncol

    fm = masked(factor[0, :, 0, :, 0], pattern[0, :, 0, :, 0])
    lm = masked(lower_bridge[0, :, 0, :, 0], lower_links[0, :, 0, :, 0])
    um = masked(upper_bridge[0, :, 0, :, 0], upper_links[0, :, 0, :, 0])
    tm = masked(top_factor[:, 0, :, 0], top_pattern[:, 0, :, 0])
    marks = lax.broadcasted_iota(jnp.int32, (levels, block, 1), 1)
    keep = (marks < widths[0, :, 0][:, None, None]).astype(f32)
    chip_start = (lax.axis_index("col") // 2) * share
    own_rhs = lax.dynamic_slice_in_dim(own_half(rhs[0, :, 0], ncol), chip_start, share, 2)
    inv = factor_inv[0, :, :, 0]
    top_rhs = lax.dynamic_slice_in_dim(own_half(rhs_top[:, 0], ncol), chip_start, share, 2)
    tinv = top_inv[:, :, 0]

    ys = []
    segs = []
    for level in range(levels):
        if level == 0:
            resid = own_rhs[0].astype(bf16)
        else:
            part = products([fm[level, j] for j in range(level)], segs)
            resid = (own_rhs[level] - column_chunk_total(part, ncol)).astype(bf16)
        solved = keep[level] * jnp.dot(inv[0, level], resid, preferred_element_type=f32)
        ys.append(solved)
        segs.append(to_columns(join_chunks(solved.astype(bf16), ncol), n))

    coupling = [column_chunk_total(products([lm[t, j] for j in range(levels)], segs), ncol, leaves) for t in range(tops)]

    yts = []
    tsegs = []
    for top in range(tops):
        summed = coupling[top]
        if top > 0:
            part = products([tm[top, j] for j in range(top)], tsegs)
            summed = summed + column_chunk_total(part, ncol)
        resid = (top_rhs[top] - summed).astype(bf16)
        solved = jnp.dot(tinv[0, top], resid, preferred_element_type=f32)
        yts.append(solved)
        tsegs.append(to_columns(join_chunks(solved.astype(bf16), ncol), n))

    zts = [None] * tops
    tback = [None] * tops
    for top in reversed(range(tops)):
        if top == tops - 1:
            resid = yts[top].astype(bf16)
        else:
            part = products([tm[top, j] for j in range(top + 1, tops)], tback[top + 1 :])
            resid = (yts[top] - column_chunk_total(part, ncol)).astype(bf16)
        solved = jnp.dot(tinv[1, top], resid, preferred_element_type=f32)
        zts[top] = solved
        tback[top] = to_columns(join_chunks(solved.astype(bf16), ncol), n)

    zs = [None] * levels
    back = [None] * levels
    for level in reversed(range(levels)):
        blocks = [um[level, t] for t in range(tops)] + [fm[level, j] for j in range(level + 1, levels)]
        part = products(blocks, tback + back[level + 1 :])
        resid = (ys[level] - column_chunk_total(part, ncol)).astype(bf16)
        solved = keep[level] * jnp.dot(inv[1, level], resid, preferred_element_type=f32)
        zs[level] = solved
        if level > 0:
            back[level] = to_columns(join_chunks(solved.astype(bf16), ncol), n)

    result = jnp.stack(zs, 0)
    result_top = jnp.stack(zts, 0)
    return (result[None, :, None], result_top[:, None])


def solution(mesh):
    assert mesh.shape["row"] == mesh.shape["col"]
    placed = (
        P("leaf", None, "row", None, None),
        P(None, "row", None, None),
        P("leaf", None, "row", None, "col", None, None),
        P("leaf", None, None, "row", None, None),
        P("leaf", None, "row", None, "col", None, None),
        P("leaf", None, "row", None, "col", None, None),
        P(None, "row", None, "col", None, None),
        P(None, None, "row", None, None),
        P("leaf", None, "row"),
        P("leaf", None, "row", None, "col"),
        P("leaf", None, "row", None, "col"),
        P("leaf", None, "row", None, "col"),
        P(None, "row", None, "col"),
    )
    return jax.shard_map(
        shards,
        mesh=mesh,
        in_specs=placed,
        out_specs=(P("leaf", None, "row", None, "col"), P(None, "row", None, "col")),
        check_vma=False,
    )
```
